1024 devices in a mesh: row: 128 (over z, x, core), vec: 8 (over y).
Axes of the slice: x: 8, y: 8, z: 8, core: 2. Of those that a mesh axis runs over, the one named last changes fastest.
Arguments:
- vectors: bfloat16 [131072, 1024], P(('row', 'vec')), may hold values from -6 to 6
- rotation: bfloat16 [1024, 1024], replicated, may hold values from -0.1875 to 0.1875
- blocks: bfloat16 [1024, 8, 128, 128], P('row'), may hold values from -0.1875 to 0.1875
- columns: int32 [1024, 8], P('row'), may hold values from 0 to 1023, as said below
Outputs:
- filtered: bfloat16 [131072, 1024], P('row', 'vec')
The draws below stay inside these ranges and needn't reach their ends.
Inputs may be any that keep to these rules, and one draw needn't show every extreme that they name: `columns`: block row i stores its own block first, then block max(i - 6, 0), then block min(i + 2, 1023); every other entry lies between i - 6 and i + 2, clipped to the grid.
All inputs are finite; a program needn't handle non-finite values.
Results may differ from the reference program's by a relative error of at most 0.0065.
Values may be sent and summed in bfloat16 or wider, within the bound.
No kernel may reach another device: no remote copies, remote signals or barrier semaphores. Data moves between devices by JAX's collectives and lax.ppermute only.
A program may use at most 32 MiB of HBM per device.

```python
import jax
import jax.numpy as jnp
from jax import lax

BS = 128
NV = 1024
NNZ = 8
DEG = 4
REACH_LO = 6
REACH_HI = 2
NB = 1024
NROWS = 131072


def draw_columns(key, part):
    own = jnp.arange(NB, dtype=jnp.int32)[:, None]
    offsets = jax.random.randint(key, (NB, NNZ - 3), -REACH_LO, REACH_HI + 1).astype(jnp.int32)
    fixed_part = jnp.concatenate([own, own - REACH_LO, own + REACH_HI], axis=1)
    whole = jnp.concatenate([fixed_part, own + offsets], axis=1)
    return jnp.clip(whole, 0, NB - 1).astype(jnp.int32)


def level_of(own_key, extent, cuts, smallest, largest):
    level, own = 1.0, jax.random.fold_in(own_key, 6)
    for dim, shards_of in cuts:
        heights = jnp.exp(jax.random.uniform(jax.random.fold_in(own, dim), (shards_of,), jnp.float32, smallest / len(cuts), largest / len(cuts)))
        level = level * jnp.repeat(heights, extent[dim] // shards_of).reshape([-1 if axis == dim else 1 for axis in range(len(extent))])
    return level


def normal_values(own_key, extent, deviation, reach, split=(), kind=jnp.bfloat16):
    drawn = jax.random.normal(own_key, extent, jnp.float32) * deviation
    if len(split) > 0:
        drawn = level_of(own_key, extent, split, -0.22, 0.18) * drawn
    return jnp.clip(drawn, min=-reach, max=reach).astype(kind)


def setup_inputs(seed: int = 0) -> dict:
    key_list = jax.random.split(jax.random.key(seed), 5)
    return {
        "vectors": normal_values(key_list[0], (NROWS, NV), 1.0, 6.0, ((0, 1024),)),
        "rotation": normal_values(key_list[1], (NV, NV), NV ** -0.5, 0.1875),
        "blocks": normal_values(key_list[2], (NB, NNZ, BS, BS), (NNZ * BS) ** -0.5, 0.1875, ((0, 128),)),
        "columns": draw_columns(jax.random.fold_in(key_list[4], 71), 0),
    }


def apply_operator(blocks, columns, state_bf):
    tiles = state_bf.reshape(NB, BS, NV)

    def add_entry(total, entry):
        picked = tiles[columns[:, entry]].astype(jnp.float32)
        tile_ops = blocks[:, entry].astype(jnp.float32)
        return total + jnp.einsum('brc,bcv->brv', tile_ops, picked), None

    start = jnp.zeros((NB, BS, NV), jnp.float32)
    total, unused = lax.scan(add_entry, start, jnp.arange(NNZ))
    return total.reshape(NROWS, NV)


def reference(vectors, rotation, blocks, columns):
    rotated = jnp.dot(vectors, rotation, preferred_element_type=jnp.float32).astype(jnp.bfloat16)
    prev = rotated.astype(jnp.float32)
    cur = (apply_operator(blocks, columns, rotated) - 0.25 * prev) / 2.0
    for degree in range(DEG - 1):
        sent = cur.astype(jnp.bfloat16)
        nxt = 2.0 * (apply_operator(blocks, columns, sent) - 0.25 * cur) / 2.0 - prev
        prev = cur
        cur = nxt
    return cur.astype(jnp.bfloat16)
```

```python
import jax
import jax.numpy as jnp
from jax import lax
from jax.experimental import pallas as pl
from jax.experimental.pallas import tpu as pltpu
from jax.sharding import PartitionSpec as P

DEG = 4
REACH_LO = 6
REACH_HI = 2


def shift_up(cells, axis):
    count = lax.axis_size(axis)
    return lax.ppermute(cells, axis, [(i, i + 1) for i in range(count - 1)])


def shift_down(cells, axis):
    count = lax.axis_size(axis)
    return lax.ppermute(cells, axis, [(i + 1, i) for i in range(count - 1)])


def halo_extend(state_bf, block_rows):
    lo = shift_up(state_bf[state_bf.shape[0] - REACH_LO * block_rows:], "row")
    hi = shift_down(state_bf[: REACH_HI * block_rows], "row")
    return jnp.concatenate([lo, state_bf, hi], axis=0)


def make_apply(local_blocks, nnz, block_rows, width, n_tiles, first):
    def kernel(idx_ref, ext_ref, blk_ref, *rest):
        if first:
            cur_out, sent_out = rest
        else:
            cur_ref, prev_ref, cur_out, sent_out = rest

        def row_body(b, carry):
            acc = jnp.zeros((block_rows, width), jnp.float32)
            for j in range(nnz):
                t = idx_ref[b * nnz + j]
                acc = acc + jnp.dot(blk_ref[b, j], ext_ref[t], preferred_element_type=jnp.float32)
            if first:
                p = ext_ref[b + REACH_LO].astype(jnp.float32)
                nxt = (acc - 0.25 * p) / 2.0
            else:
                c = cur_ref[b]
                nxt = 2.0 * (acc - 0.25 * c) / 2.0 - prev_ref[b]
            cur_out[b] = nxt
            sent_out[b] = nxt.astype(jnp.bfloat16)
            return carry

        lax.fori_loop(0, local_blocks, row_body, 0)

    vmem = pl.BlockSpec(memory_space=pltpu.VMEM)
    smem = pl.BlockSpec(memory_space=pltpu.SMEM)
    n_in = 3 if first else 5
    shape3 = (local_blocks, block_rows, width)
    return pl.pallas_call(
        kernel,
        in_specs=[smem] + [vmem] * (n_in - 1),
        out_specs=(vmem, vmem),
        out_shape=(
            jax.ShapeDtypeStruct(shape3, jnp.float32),
            jax.ShapeDtypeStruct(shape3, jnp.bfloat16),
        ),
    )


def per_device(vectors, rotation, blocks, columns):
    rotated = jnp.dot(vectors, rotation, preferred_element_type=jnp.float32).astype(jnp.bfloat16)
    panel = lax.all_to_all(rotated, "vec", split_axis=1, concat_axis=0, tiled=True)
    local_blocks, nnz, block_rows, _ = blocks.shape
    width = panel.shape[1]
    n_tiles = local_blocks + REACH_LO + REACH_HI
    first_block = lax.axis_index("row") * local_blocks
    local_index = jnp.clip(columns - first_block + REACH_LO, 0, n_tiles - 1).reshape(-1).astype(jnp.int32)

    first_apply = make_apply(local_blocks, nnz, block_rows, width, n_tiles, True)
    next_apply = make_apply(local_blocks, nnz, block_rows, width, n_tiles, False)

    def tiles_of(state_bf):
        return halo_extend(state_bf, block_rows).reshape(n_tiles, block_rows, width)

    prev = panel.astype(jnp.float32).reshape(local_blocks, block_rows, width)
    cur, sent = first_apply(local_index, tiles_of(panel), blocks)
    for degree in range(DEG - 1):
        nxt, sent = next_apply(local_index, tiles_of(sent.reshape(-1, width)), blocks, cur, prev)
        prev = cur
        cur = nxt
    return sent.reshape(local_blocks * block_rows, width)


def solution(mesh):
    return jax.shard_map(
        per_device,
        mesh=mesh,
        in_specs=(P(("row", "vec"), None), P(), P("row", None, None, None), P("row", None)),
        out_specs=P("row", "vec"),
        check_vma=False,
    )
```

```python
import jax
import jax.numpy as jnp
from jax import lax
from jax.experimental import pallas as pl
from jax.experimental.pallas import tpu as pltpu
from jax.sharding import PartitionSpec as P

DEG = 4
REACH_LO = 6
REACH_HI = 2


def shift_up(cells, axis):
    count = lax.axis_size(axis)
    return lax.ppermute(cells, axis, [(i, i + 1) for i in range(count - 1)])


def shift_down(cells, axis):
    count = lax.axis_size(axis)
    return lax.ppermute(cells, axis, [(i + 1, i) for i in range(count - 1)])


def make_apply(local_blocks, nnz, block_rows, width, piece_sizes, first, last):
    n_pieces = len(piece_sizes)
    n_tiles = sum(piece_sizes)
    n_in = n_pieces + 1 + (0 if first else 2)
    out_split = (local_blocks,) if last else (REACH_HI, local_blocks - REACH_HI)
    n_out = len(out_split) + (0 if last else 1)
    f32, bf16 = jnp.float32, jnp.bfloat16

    def kernel(idx_ref, *refs):
        ins = refs[:n_in]
        outs = refs[n_in:n_in + n_out]
        ext_v, blk_v, cp_v, res_v, sent_v, in_sem, blk_sem, cp_sem, out_sem = refs[n_in + n_out:]
        pieces = ins[:n_pieces]
        blk_hbm = ins[n_pieces]

        ext_copies = []
        start = 0
        for k, size in enumerate(piece_sizes):
            ext_copies.append(pltpu.make_async_copy(pieces[k], ext_v.at[start:start + size], in_sem.at[k]))
            start += size
        blk_copies = [pltpu.make_async_copy(blk_hbm.at[b], blk_v.at[b], blk_sem.at[b]) for b in range(local_blocks)]
        cp_copies = []
        if not first:
            cp_copies = [pltpu.make_async_copy(ins[n_pieces + 1 + k], cp_v.at[k], cp_sem.at[k]) for k in range(2)]
        for c in ext_copies:
            c.start()
        for c in blk_copies:
            c.start()
        for c in cp_copies:
            c.start()
        for c in ext_copies:
            c.wait()
        for c in cp_copies:
            c.wait()

        out_copies = []
        for b in range(local_blocks):
            blk_copies[b].wait()
            acc = jnp.zeros((block_rows, width), f32)
            for j in range(nnz):
                t = idx_ref[b * nnz + j]
                acc = acc + jnp.dot(blk_v[b, j], ext_v[t], preferred_element_type=f32)
            if first:
                p = ext_v[b + REACH_LO].astype(f32)
                nxt = (acc - 0.25 * p) / 2.0
            else:
                nxt = 2.0 * (acc - 0.25 * cp_v[0, b]) / 2.0 - cp_v[1, b]
            sent_v[b] = nxt.astype(bf16)
            if not last:
                res_v[b] = nxt
                c = pltpu.make_async_copy(res_v.at[b], outs[0].at[b], out_sem.at[b])
                c.start()
                out_copies.append(c)
        base = 0 if last else 1
        start = 0
        for k, size in enumerate(out_split):
            c = pltpu.make_async_copy(sent_v.at[start:start + size], outs[base + k], out_sem.at[local_blocks + k])
            c.start()
            out_copies.append(c)
            start += size
        for c in out_copies:
            c.wait()

    any_spec = pl.BlockSpec(memory_space=pl.ANY)
    smem = pl.BlockSpec(memory_space=pltpu.SMEM)
    out_shape = []
    if not last:
        out_shape.append(jax.ShapeDtypeStruct((local_blocks, block_rows, width), f32))
    for size in out_split:
        out_shape.append(jax.ShapeDtypeStruct((size, block_rows, width), bf16))
    return pl.pallas_call(
        kernel,
        in_specs=[smem] + [any_spec] * n_in,
        out_specs=tuple([any_spec] * n_out),
        out_shape=tuple(out_shape),
        scratch_shapes=[
            pltpu.VMEM((n_tiles, block_rows, width), bf16),
            pltpu.VMEM((local_blocks, nnz, block_rows, block_rows), bf16),
            pltpu.VMEM((2, local_blocks, block_rows, width), f32),
            pltpu.VMEM((local_blocks, block_rows, width), f32),
            pltpu.VMEM((local_blocks, block_rows, width), bf16),
            pltpu.SemaphoreType.DMA((n_pieces,)),
            pltpu.SemaphoreType.DMA((local_blocks,)),
            pltpu.SemaphoreType.DMA((2,)),
            pltpu.SemaphoreType.DMA((local_blocks + 2,)),
        ],
    )


def per_device(vectors, rotation, blocks, columns):
    rotated = jnp.dot(vectors, rotation, preferred_element_type=jnp.float32).astype(jnp.bfloat16)
    panel = lax.all_to_all(rotated, "vec", split_axis=1, concat_axis=0, tiled=True)
    local_blocks, nnz, block_rows, _ = blocks.shape
    width = panel.shape[1]
    n_tiles = local_blocks + REACH_LO + REACH_HI
    first_block = lax.axis_index("row") * local_blocks
    local_index = jnp.clip(columns - first_block + REACH_LO, 0, n_tiles - 1).reshape(-1).astype(jnp.int32)

    tiles = panel.reshape(local_blocks, block_rows, width)
    head = tiles[:REACH_HI]
    tail = tiles[local_blocks - REACH_LO:]
    sizes_first = (REACH_LO, local_blocks, REACH_HI)
    sizes_next = (REACH_LO, REACH_HI, local_blocks - REACH_HI, REACH_HI)
    first_apply = make_apply(local_blocks, nnz, block_rows, width, sizes_first, True, False)
    next_apply = make_apply(local_blocks, nnz, block_rows, width, sizes_next, False, False)
    last_apply = make_apply(local_blocks, nnz, block_rows, width, sizes_next, False, True)

    prev = tiles.astype(jnp.float32)
    cur, head, rest = first_apply(local_index, shift_up(tail, "row"), tiles, shift_down(head, "row"), blocks)
    for degree in range(DEG - 1):
        tail = rest[rest.shape[0] - REACH_LO:]
        lo = shift_up(tail, "row")
        hi = shift_down(head, "row")
        if degree < DEG - 2:
            nxt, head, rest = next_apply(local_index, lo, head, rest, hi, blocks, cur, prev)
            prev = cur
            cur = nxt
        else:
            (out,) = last_apply(local_index, lo, head, rest, hi, blocks, cur, prev)
    return out.reshape(local_blocks * block_rows, width)


def solution(mesh):
    return jax.shard_map(
        per_device,
        mesh=mesh,
        in_specs=(P(("row", "vec"), None), P(), P("row", None, None, None), P("row", None)),
        out_specs=P("row", "vec"),
        check_vma=False,
    )
```

```python
import jax
import jax.numpy as jnp
from jax import lax
from jax.experimental import pallas as pl
from jax.experimental.pallas import tpu as pltpu
from jax.sharding import PartitionSpec as P

DEG = 4
REACH_LO = 6
REACH_HI = 2


def shift_up(cells, axis):
    count = lax.axis_size(axis)
    return lax.ppermute(cells, axis, [(i, i + 1) for i in range(count - 1)])


def shift_down(cells, axis):
    count = lax.axis_size(axis)
    return lax.ppermute(cells, axis, [(i + 1, i) for i in range(count - 1)])


def make_apply(local_blocks, nnz, block_rows, width, piece_sizes, first, last, prev_bf16=False):
    n_pieces = len(piece_sizes)
    n_tiles = sum(piece_sizes)
    n_in = n_pieces + 1 + (0 if first else 2)
    out_split = (local_blocks,) if last else (REACH_HI, local_blocks - REACH_HI)
    n_out = len(out_split) + (0 if last else 1)
    f32, bf16 = jnp.float32, jnp.bfloat16

    def kernel(idx_ref, *refs):
        ins = refs[:n_in]
        outs = refs[n_in:n_in + n_out]
        ext_v, blk_v, cur_v, prev_v, res_v, sent_v, in_sem, blk_sem, cp_sem, out_sem = refs[n_in + n_out:]
        pieces = ins[:n_pieces]
        blk_hbm = ins[n_pieces]

        ext_copies = []
        start = 0
        for k, size in enumerate(piece_sizes):
            ext_copies.append(pltpu.make_async_copy(pieces[k], ext_v.at[start:start + size], in_sem.at[k]))
            start += size
        blk_copies = [pltpu.make_async_copy(blk_hbm.at[b], blk_v.at[b], blk_sem.at[b]) for b in range(local_blocks)]
        cp_copies = []
        if not first:
            cp_copies = [
                pltpu.make_async_copy(ins[n_pieces + 1], cur_v, cp_sem.at[0]),
                pltpu.make_async_copy(ins[n_pieces + 2], prev_v, cp_sem.at[1]),
            ]
        for c in ext_copies:
            c.start()
        for c in blk_copies:
            c.start()
        for c in cp_copies:
            c.start()
        for c in ext_copies:
            c.wait()
        for c in cp_copies:
            c.wait()

        out_copies = []
        for b in range(local_blocks):
            blk_copies[b].wait()
            lhs = jnp.concatenate([blk_v[b, j] for j in range(nnz)], axis=1)
            rhs = jnp.concatenate([ext_v[idx_ref[b * nnz + j]] for j in range(nnz)], axis=0)
            acc = jnp.dot(lhs, rhs, preferred_element_type=f32)
            if first:
                p = ext_v[b + REACH_LO].astype(f32)
                nxt = (acc - 0.25 * p) / 2.0
            else:
                nxt = 2.0 * (acc - 0.25 * cur_v[b]) / 2.0 - prev_v[b].astype(f32)
            sent_v[b] = nxt.astype(bf16)
            if not last:
                res_v[b] = nxt
                c = pltpu.make_async_copy(res_v.at[b], outs[0].at[b], out_sem.at[b])
                c.start()
                out_copies.append(c)
        base = 0 if last else 1
        start = 0
        for k, size in enumerate(out_split):
            c = pltpu.make_async_copy(sent_v.at[start:start + size], outs[base + k], out_sem.at[local_blocks + k])
            c.start()
            out_copies.append(c)
            start += size
        for c in out_copies:
            c.wait()

    any_spec = pl.BlockSpec(memory_space=pl.ANY)
    smem = pl.BlockSpec(memory_space=pltpu.SMEM)
    out_shape = []
    if not last:
        out_shape.append(jax.ShapeDtypeStruct((local_blocks, block_rows, width), f32))
    for size in out_split:
        out_shape.append(jax.ShapeDtypeStruct((size, block_rows, width), bf16))
    return pl.pallas_call(
        kernel,
        in_specs=[smem] + [any_spec] * n_in,
        out_specs=tuple([any_spec] * n_out),
        out_shape=tuple(out_shape),
        scratch_shapes=[
            pltpu.VMEM((n_tiles, block_rows, width), bf16),
            pltpu.VMEM((local_blocks, nnz, block_rows, block_rows), bf16),
            pltpu.VMEM((local_blocks, block_rows, width), f32),
            pltpu.VMEM((local_blocks, block_rows, width), bf16 if prev_bf16 else f32),
            pltpu.VMEM((local_blocks, block_rows, width), f32),
            pltpu.VMEM((local_blocks, block_rows, width), bf16),
            pltpu.SemaphoreType.DMA((n_pieces,)),
            pltpu.SemaphoreType.DMA((local_blocks,)),
            pltpu.SemaphoreType.DMA((2,)),
            pltpu.SemaphoreType.DMA((local_blocks + 2,)),
        ],
    )


def per_device(vectors, rotation, blocks, columns):
    groups = lax.axis_size("vec")
    width = rotation.shape[1] // groups
    rot3 = rotation.reshape(rotation.shape[0], groups, width)
    rotated = jnp.einsum("rk,kgc->grc", vectors, rot3, preferred_element_type=jnp.float32).astype(jnp.bfloat16)
    panel = lax.all_to_all(rotated, "vec", split_axis=0, concat_axis=0, tiled=True)
    local_blocks, nnz, block_rows, _ = blocks.shape
    n_tiles = local_blocks + REACH_LO + REACH_HI
    first_block = lax.axis_index("row") * local_blocks
    local_index = jnp.clip(columns - first_block + REACH_LO, 0, n_tiles - 1).reshape(-1).astype(jnp.int32)

    tiles = panel.reshape(local_blocks, block_rows, width)
    head = tiles[:REACH_HI]
    tail = tiles[local_blocks - REACH_LO:]
    sizes_first = (REACH_LO, local_blocks, REACH_HI)
    sizes_next = (REACH_LO, REACH_HI, local_blocks - REACH_HI, REACH_HI)
    first_apply = make_apply(local_blocks, nnz, block_rows, width, sizes_first, True, False)
    second_apply = make_apply(local_blocks, nnz, block_rows, width, sizes_next, False, False, True)
    next_apply = make_apply(local_blocks, nnz, block_rows, width, sizes_next, False, False)
    last_apply = make_apply(local_blocks, nnz, block_rows, width, sizes_next, False, True)

    prev = tiles
    cur, head, rest = first_apply(local_index, shift_up(tail, "row"), tiles, shift_down(head, "row"), blocks)
    for degree in range(DEG - 1):
        tail = rest[rest.shape[0] - REACH_LO:]
        lo = shift_up(tail, "row")
        hi = shift_down(head, "row")
        if degree < DEG - 2:
            step = second_apply if degree == 0 else next_apply
            nxt, head, rest = step(local_index, lo, head, rest, hi, blocks, cur, prev)
            prev = cur
            cur = nxt
        else:
            (out,) = last_apply(local_index, lo, head, rest, hi, blocks, cur, prev)
    return out.reshape(local_blocks * block_rows, width)


def solution(mesh):
    return jax.shard_map(
        per_device,
        mesh=mesh,
        in_specs=(P(("row", "vec"), None), P(), P("row", None, None, None), P("row", None)),
        out_specs=P("row", "vec"),
        check_vma=False,
    )
```

```python
import jax
import jax.numpy as jnp
from jax import lax
from jax.sharding import PartitionSpec as P

DEG = 4
REACH_LO = 6
REACH_HI = 2
CHUNKS = 1


def shift_up(cells, axis):
    count = lax.axis_size(axis)
    return lax.ppermute(cells, axis, [(i, i + 1) for i in range(count - 1)])


def shift_down(cells, axis):
    count = lax.axis_size(axis)
    return lax.ppermute(cells, axis, [(i + 1, i) for i in range(count - 1)])


def filter_chunk(panel, blocks, local_index):
    local_blocks, nnz, block_rows, _ = blocks.shape
    width = panel.shape[1]

    def apply_operator(state_bf):
        lo = shift_up(state_bf[state_bf.shape[0] - REACH_LO * block_rows:], "row")
        hi = shift_down(state_bf[: REACH_HI * block_rows], "row")
        tiles = jnp.concatenate([lo, state_bf, hi], axis=0).reshape(-1, block_rows, width)
        picked = tiles[local_index]
        result = jnp.einsum("bjrc,bjcv->brv", blocks, picked, preferred_element_type=jnp.float32)
        return result.reshape(local_blocks * block_rows, width)

    prev = panel.astype(jnp.float32)
    cur = (apply_operator(panel) - 0.25 * prev) / 2.0
    for degree in range(DEG - 1):
        sent = cur.astype(jnp.bfloat16)
        nxt = 2.0 * (apply_operator(sent) - 0.25 * cur) / 2.0 - prev
        prev = cur
        cur = nxt
    return cur.astype(jnp.bfloat16)


def per_device(vectors, rotation, blocks, columns):
    rotated = jnp.dot(vectors, rotation, preferred_element_type=jnp.float32).astype(jnp.bfloat16)
    panel = lax.all_to_all(rotated, "vec", split_axis=1, concat_axis=0, tiled=True)
    local_blocks = blocks.shape[0]
    n_tiles = local_blocks + REACH_LO + REACH_HI
    first_block = lax.axis_index("row") * local_blocks
    local_index = jnp.clip(columns - first_block + REACH_LO, 0, n_tiles - 1)
    width = panel.shape[1] // CHUNKS
    outs = [filter_chunk(panel[:, k * width:(k + 1) * width], blocks, local_index) for k in range(CHUNKS)]
    return outs[0] if CHUNKS == 1 else jnp.concatenate(outs, axis=1)


def solution(mesh):
    return jax.shard_map(
        per_device,
        mesh=mesh,
        in_specs=(P(("row", "vec"), None), P(), P("row", None, None, None), P("row", None)),
        out_specs=P("row", "vec"),
        check_vma=False,
    )
```

```python
import jax
import jax.numpy as jnp
from jax import lax
from jax.sharding import PartitionSpec as P

DEG = 4
REACH_LO = 6
REACH_HI = 2
CHUNKS = 2


def shift_up(cells, axis):
    count = lax.axis_size(axis)
    return lax.ppermute(cells, axis, [(i, i + 1) for i in range(count - 1)])


def shift_down(cells, axis):
    count = lax.axis_size(axis)
    return lax.ppermute(cells, axis, [(i + 1, i) for i in range(count - 1)])


def filter_chunk(panel, blocks, local_index):
    local_blocks, nnz, block_rows, _ = blocks.shape
    width = panel.shape[1]

    def apply_operator(state_bf):
        lo = shift_up(state_bf[state_bf.shape[0] - REACH_LO * block_rows:], "row")
        hi = shift_down(state_bf[: REACH_HI * block_rows], "row")
        tiles = jnp.concatenate([lo, state_bf, hi], axis=0).reshape(-1, block_rows, width)
        picked = tiles[local_index]
        result = jnp.einsum("bjrc,bjcv->brv", blocks, picked, preferred_element_type=jnp.float32)
        return result.reshape(local_blocks * block_rows, width)

    prev = panel.astype(jnp.float32)
    cur = (apply_operator(panel) - 0.25 * prev) / 2.0
    for degree in range(DEG - 1):
        sent = cur.astype(jnp.bfloat16)
        nxt = 2.0 * (apply_operator(sent) - 0.25 * cur) / 2.0 - prev
        prev = cur
        cur = nxt
    return cur.astype(jnp.bfloat16)


def per_device(vectors, rotation, blocks, columns):
    rotated = jnp.dot(vectors, rotation, preferred_element_type=jnp.float32).astype(jnp.bfloat16)
    panel = lax.all_to_all(rotated, "vec", split_axis=1, concat_axis=0, tiled=True)
    local_blocks = blocks.shape[0]
    n_tiles = local_blocks + REACH_LO + REACH_HI
    first_block = lax.axis_index("row") * local_blocks
    local_index = jnp.clip(columns - first_block + REACH_LO, 0, n_tiles - 1)
    width = panel.shape[1] // CHUNKS
    outs = [filter_chunk(panel[:, k * width:(k + 1) * width], blocks, local_index) for k in range(CHUNKS)]
    return outs[0] if CHUNKS == 1 else jnp.concatenate(outs, axis=1)


def solution(mesh):
    return jax.shard_map(
        per_device,
        mesh=mesh,
        in_specs=(P(("row", "vec"), None), P(), P("row", None, None, None), P("row", None)),
        out_specs=P("row", "vec"),
        check_vma=False,
    )
```

```python
import jax
import jax.numpy as jnp
from jax import lax
from jax.sharding import PartitionSpec as P

DEG = 4
REACH_LO = 6
REACH_HI = 2


def shift_up(cells, axis):
    count = lax.axis_size(axis)
    return lax.ppermute(cells, axis, [(i, i + 1) for i in range(count - 1)])


def shift_down(cells, axis):
    count = lax.axis_size(axis)
    return lax.ppermute(cells, axis, [(i + 1, i) for i in range(count - 1)])


def filter_chunk(panel, first_tiles, blocks, local_index):
    local_blocks, nnz, block_rows, _ = blocks.shape
    width = panel.shape[1]

    def product(tiles):
        picked = tiles[local_index]
        result = jnp.einsum("bjrc,bjcv->brv", blocks, picked, preferred_element_type=jnp.float32)
        return result.reshape(local_blocks * block_rows, width)

    def apply_operator(state_bf):
        lo = shift_up(state_bf[state_bf.shape[0] - REACH_LO * block_rows:], "row")
        hi = shift_down(state_bf[: REACH_HI * block_rows], "row")
        return product(jnp.concatenate([lo, state_bf, hi], axis=0).reshape(-1, block_rows, width))

    prev = panel.astype(jnp.float32)
    cur = (product(first_tiles) - 0.25 * prev) / 2.0
    for degree in range(DEG - 1):
        sent = cur.astype(jnp.bfloat16)
        nxt = 2.0 * (apply_operator(sent) - 0.25 * cur) / 2.0 - prev
        prev = cur
        cur = nxt
    return cur.astype(jnp.bfloat16)


def neighbour_rows(vectors, rows, groups, block_rows):
    pairs = []
    for r in range(rows):
        for t in range(groups):
            target = r + 1 if t >= REACH_HI else r - 1
            if 0 <= target < rows:
                pairs.append((r * groups + t, target * groups + t))
    return lax.ppermute(vectors, ("row", "vec"), pairs)


def per_device(vectors, rotation, blocks, columns):
    rows = lax.axis_size("row")
    groups = lax.axis_size("vec")
    local_blocks, nnz, block_rows, _ = blocks.shape
    width = rotation.shape[1] // groups
    both = jnp.concatenate([vectors, neighbour_rows(vectors, rows, groups, block_rows)], axis=0)
    rotated = jnp.dot(both, rotation, preferred_element_type=jnp.float32).astype(jnp.bfloat16)
    spread = rotated.reshape(2, block_rows, groups, width)
    got = lax.all_to_all(spread, "vec", split_axis=2, concat_axis=2, tiled=True)
    got = got.transpose(0, 2, 1, 3)
    panel = got[0].reshape(local_blocks * block_rows, width)
    first_tiles = jnp.concatenate([got[1, REACH_HI:], got[0], got[1, :REACH_HI]], axis=0)
    n_tiles = local_blocks + REACH_LO + REACH_HI
    first_block = lax.axis_index("row") * local_blocks
    local_index = jnp.clip(columns - first_block + REACH_LO, 0, n_tiles - 1)
    return filter_chunk(panel, first_tiles, blocks, local_index)


def solution(mesh):
    return jax.shard_map(
        per_device,
        mesh=mesh,
        in_specs=(P(("row", "vec"), None), P(), P("row", None, None, None), P("row", None)),
        out_specs=P("row", "vec"),
        check_vma=False,
    )
```

```python
import jax
import jax.numpy as jnp
from jax import lax
from jax.sharding import PartitionSpec as P

DEG = 4
REACH_LO = 6
REACH_HI = 2
CHUNKS = 1


def shift_up(cells, axis):
    count = lax.axis_size(axis)
    return lax.ppermute(cells, axis, [(i, i + 1) for i in range(count - 1)])


def shift_down(cells, axis):
    count = lax.axis_size(axis)
    return lax.ppermute(cells, axis, [(i + 1, i) for i in range(count - 1)])


def filter_chunk(panel, blocks, local_index):
    local_blocks, nnz, block_rows, _ = blocks.shape
    width = panel.shape[1]

    def apply_operator(state_bf):
        lo = shift_up(state_bf[state_bf.shape[0] - REACH_LO * block_rows:], "row")
        hi = shift_down(state_bf[: REACH_HI * block_rows], "row")
        tiles = jnp.concatenate([lo, state_bf, hi], axis=0).reshape(-1, block_rows, width)
        picked = tiles[local_index]
        result = jnp.einsum("bjrc,bjcv->brv", blocks, picked, preferred_element_type=jnp.float32)
        return result.reshape(local_blocks * block_rows, width)

    prev = panel.astype(jnp.float32)
    cur = (apply_operator(panel) - 0.25 * prev) / 2.0
    for degree in range(DEG - 1):
        sent = cur.astype(jnp.bfloat16)
        nxt = 2.0 * (apply_operator(sent) - 0.25 * cur) / 2.0 - prev
        prev = cur
        cur = nxt
    return cur.astype(jnp.bfloat16)


def exchange_groups(rotated, axis):
    count = lax.axis_size(axis)
    v = lax.axis_index(axis)
    width = rotated.shape[1] // count
    rows = rotated.shape[0]
    got = [lax.dynamic_slice_in_dim(rotated, v * width, width, axis=1)]
    for s in range(1, count):
        piece = lax.dynamic_slice_in_dim(rotated, ((v + s) % count) * width, width, axis=1)
        got.append(lax.ppermute(piece, axis, [(i, (i + s) % count) for i in range(count)]))
    by_shift = jnp.stack(got)
    order = (v - jnp.arange(count)) % count
    return by_shift[order].reshape(count * rows, width)


def per_device(vectors, rotation, blocks, columns):
    rotated = jnp.dot(vectors, rotation, preferred_element_type=jnp.float32).astype(jnp.bfloat16)
    panel = exchange_groups(rotated, "vec")
    local_blocks = blocks.shape[0]
    n_tiles = local_blocks + REACH_LO + REACH_HI
    first_block = lax.axis_index("row") * local_blocks
    local_index = jnp.clip(columns - first_block + REACH_LO, 0, n_tiles - 1)
    width = panel.shape[1] // CHUNKS
    outs = [filter_chunk(panel[:, k * width:(k + 1) * width], blocks, local_index) for k in range(CHUNKS)]
    return outs[0] if CHUNKS == 1 else jnp.concatenate(outs, axis=1)


def solution(mesh):
    return jax.shard_map(
        per_device,
        mesh=mesh,
        in_specs=(P(("row", "vec"), None), P(), P("row", None, None, None), P("row", None)),
        out_specs=P("row", "vec"),
        check_vma=False,
    )
```

```python
import jax
import jax.numpy as jnp
from jax import lax
from jax.sharding import PartitionSpec as P

DEG = 4
REACH_LO = 6
REACH_HI = 2
CHUNKS = 1


def shift_up(cells, axis):
    count = lax.axis_size(axis)
    return lax.ppermute(cells, axis, [(i, i + 1) for i in range(count - 1)])


def shift_down(cells, axis):
    count = lax.axis_size(axis)
    return lax.ppermute(cells, axis, [(i + 1, i) for i in range(count - 1)])


def filter_chunk(panel, blocks, local_index):
    local_blocks, nnz, block_rows, _ = blocks.shape
    width = panel.shape[1]

    row = lax.axis_index("row")
    rows = lax.axis_size("row")
    fixed_blocks = blocks[:, :3]
    free_blocks = blocks[:, 3:]
    free_index = local_index[:, 3:]

    def apply_operator(state_bf):
        lo = shift_up(state_bf[state_bf.shape[0] - REACH_LO * block_rows:], "row")
        hi = shift_down(state_bf[: REACH_HI * block_rows], "row")
        lo = jnp.where(row == 0, jnp.tile(state_bf[:block_rows], (REACH_LO, 1)), lo)
        hi = jnp.where(row == rows - 1, jnp.tile(state_bf[state_bf.shape[0] - block_rows:], (REACH_HI, 1)), hi)
        tiles = jnp.concatenate([lo, state_bf, hi], axis=0).reshape(-1, block_rows, width)
        own = tiles[REACH_LO:REACH_LO + local_blocks]
        below = tiles[:local_blocks]
        above = tiles[REACH_LO + REACH_HI:REACH_LO + REACH_HI + local_blocks]
        fixed = jnp.stack([own, below, above], axis=1)
        result = jnp.einsum("bjrc,bjcv->brv", fixed_blocks, fixed, preferred_element_type=jnp.float32)
        picked = tiles[free_index]
        result = result + jnp.einsum("bjrc,bjcv->brv", free_blocks, picked, preferred_element_type=jnp.float32)
        return result.reshape(local_blocks * block_rows, width)

    prev = panel.astype(jnp.float32)
    cur = (apply_operator(panel) - 0.25 * prev) / 2.0
    for degree in range(DEG - 1):
        sent = cur.astype(jnp.bfloat16)
        nxt = 2.0 * (apply_operator(sent) - 0.25 * cur) / 2.0 - prev
        prev = cur
        cur = nxt
    return cur.astype(jnp.bfloat16)


def per_device(vectors, rotation, blocks, columns):
    rotated = jnp.dot(vectors, rotation, preferred_element_type=jnp.float32).astype(jnp.bfloat16)
    panel = lax.all_to_all(rotated, "vec", split_axis=1, concat_axis=0, tiled=True)
    local_blocks = blocks.shape[0]
    n_tiles = local_blocks + REACH_LO + REACH_HI
    first_block = lax.axis_index("row") * local_blocks
    local_index = jnp.clip(columns - first_block + REACH_LO, 0, n_tiles - 1)
    width = panel.shape[1] // CHUNKS
    outs = [filter_chunk(panel[:, k * width:(k + 1) * width], blocks, local_index) for k in range(CHUNKS)]
    return outs[0] if CHUNKS == 1 else jnp.concatenate(outs, axis=1)


def solution(mesh):
    return jax.shard_map(
        per_device,
        mesh=mesh,
        in_specs=(P(("row", "vec"), None), P(), P("row", None, None, None), P("row", None)),
        out_specs=P("row", "vec"),
        check_vma=False,
    )
```

```python
import jax
import jax.numpy as jnp
from jax import lax
from jax.sharding import PartitionSpec as P

DEG = 4
REACH_LO = 6
REACH_HI = 2
CHUNKS = 1


def shift_up(cells, axis):
    count = lax.axis_size(axis)
    return lax.ppermute(cells, axis, [(i, i + 1) for i in range(count - 1)])


def shift_down(cells, axis):
    count = lax.axis_size(axis)
    return lax.ppermute(cells, axis, [(i + 1, i) for i in range(count - 1)])


def filter_chunk(panel, blocks, offset):
    local_blocks, nnz, block_rows, _ = blocks.shape
    width = panel.shape[1]

    def apply_operator(state_bf):
        lo = shift_up(state_bf[state_bf.shape[0] - REACH_LO * block_rows:], "row")
        hi = shift_down(state_bf[: REACH_HI * block_rows], "row")
        tiles = jnp.concatenate([lo, state_bf, hi], axis=0).reshape(-1, block_rows, width)
        picked = jnp.broadcast_to(tiles[None, :local_blocks].transpose(1, 0, 2, 3), (local_blocks, nnz, block_rows, width))
        for w in range(1, REACH_LO + REACH_HI + 1):
            window = tiles[w:w + local_blocks][:, None]
            picked = jnp.where((offset == w)[:, :, None, None], window, picked)
        result = jnp.einsum("bjrc,bjcv->brv", blocks, picked, preferred_element_type=jnp.float32)
        return result.reshape(local_blocks * block_rows, width)

    prev = panel.astype(jnp.float32)
    cur = (apply_operator(panel) - 0.25 * prev) / 2.0
    for degree in range(DEG - 1):
        sent = cur.astype(jnp.bfloat16)
        nxt = 2.0 * (apply_operator(sent) - 0.25 * cur) / 2.0 - prev
        prev = cur
        cur = nxt
    return cur.astype(jnp.bfloat16)


def per_device(vectors, rotation, blocks, columns):
    rotated = jnp.dot(vectors, rotation, preferred_element_type=jnp.float32).astype(jnp.bfloat16)
    panel = lax.all_to_all(rotated, "vec", split_axis=1, concat_axis=0, tiled=True)
    local_blocks = blocks.shape[0]
    n_tiles = local_blocks + REACH_LO + REACH_HI
    first_block = lax.axis_index("row") * local_blocks
    offset = jnp.clip(columns - first_block + REACH_LO - jnp.arange(local_blocks)[:, None], 0, REACH_LO + REACH_HI)
    width = panel.shape[1] // CHUNKS
    outs = [filter_chunk(panel[:, k * width:(k + 1) * width], blocks, offset) for k in range(CHUNKS)]
    return outs[0] if CHUNKS == 1 else jnp.concatenate(outs, axis=1)


def solution(mesh):
    return jax.shard_map(
        per_device,
        mesh=mesh,
        in_specs=(P(("row", "vec"), None), P(), P("row", None, None, None), P("row", None)),
        out_specs=P("row", "vec"),
        check_vma=False,
    )
```

```python
import jax
import jax.numpy as jnp
from jax import lax
from jax.sharding import PartitionSpec as P

DEG = 4
REACH_LO = 6
REACH_HI = 2
CHUNKS = 1


def shift_up(cells, axis):
    count = lax.axis_size(axis)
    return lax.ppermute(cells, axis, [(i, i + 1) for i in range(count - 1)])


def shift_down(cells, axis):
    count = lax.axis_size(axis)
    return lax.ppermute(cells, axis, [(i + 1, i) for i in range(count - 1)])


def filter_chunk(panel, blocks, local_index):
    local_blocks, nnz, block_rows, _ = blocks.shape
    width = panel.shape[1]

    def apply_operator(state_bf):
        lo = shift_up(state_bf[state_bf.shape[0] - REACH_LO * block_rows:], "row")
        hi = shift_down(state_bf[: REACH_HI * block_rows], "row")
        tiles = jnp.concatenate([lo, state_bf, hi], axis=0).reshape(-1, block_rows, width)
        pieces = [lax.dynamic_index_in_dim(tiles, local_index[b, j], axis=0, keepdims=False)
                  for b in range(local_blocks) for j in range(nnz)]
        picked = jnp.stack(pieces).reshape(local_blocks, nnz, block_rows, width)
        result = jnp.einsum("bjrc,bjcv->brv", blocks, picked, preferred_element_type=jnp.float32)
        return result.reshape(local_blocks * block_rows, width)

    prev = panel.astype(jnp.float32)
    cur = (apply_operator(panel) - 0.25 * prev) / 2.0
    for degree in range(DEG - 1):
        sent = cur.astype(jnp.bfloat16)
        nxt = 2.0 * (apply_operator(sent) - 0.25 * cur) / 2.0 - prev
        prev = cur
        cur = nxt
    return cur.astype(jnp.bfloat16)


def per_device(vectors, rotation, blocks, columns):
    rotated = jnp.dot(vectors, rotation, preferred_element_type=jnp.float32).astype(jnp.bfloat16)
    panel = lax.all_to_all(rotated, "vec", split_axis=1, concat_axis=0, tiled=True)
    local_blocks = blocks.shape[0]
    n_tiles = local_blocks + REACH_LO + REACH_HI
    first_block = lax.axis_index("row") * local_blocks
    local_index = jnp.clip(columns - first_block + REACH_LO, 0, n_tiles - 1)
    width = panel.shape[1] // CHUNKS
    outs = [filter_chunk(panel[:, k * width:(k + 1) * width], blocks, local_index) for k in range(CHUNKS)]
    return outs[0] if CHUNKS == 1 else jnp.concatenate(outs, axis=1)


def solution(mesh):
    return jax.shard_map(
        per_device,
        mesh=mesh,
        in_specs=(P(("row", "vec"), None), P(), P("row", None, None, None), P("row", None)),
        out_specs=P("row", "vec"),
        check_vma=False,
    )
```

```python
import jax
import jax.numpy as jnp
from jax import lax
from jax.sharding import PartitionSpec as P

DEG = 4
REACH_LO = 6
REACH_HI = 2
CHUNKS = 1


def shift_up(cells, axis):
    count = lax.axis_size(axis)
    return lax.ppermute(cells, axis, [(i, i + 1) for i in range(count - 1)])


def shift_down(cells, axis):
    count = lax.axis_size(axis)
    return lax.ppermute(cells, axis, [(i + 1, i) for i in range(count - 1)])


def filter_chunk(panel, blocks, offset):
    local_blocks, nnz, block_rows, _ = blocks.shape
    width = panel.shape[1]

    def apply_operator(state_bf):
        lo = shift_up(state_bf[state_bf.shape[0] - REACH_LO * block_rows:], "row")
        hi = shift_down(state_bf[: REACH_HI * block_rows], "row")
        tiles = jnp.concatenate([lo, state_bf, hi], axis=0).reshape(-1, block_rows, width)
        windows = [tiles[w:w + local_blocks][:, None] for w in range(REACH_LO + REACH_HI + 1)]

        def pick(first, count, candidates):
            part = offset[:, first:first + count, None, None]
            got = jnp.broadcast_to(windows[candidates[0]], (local_blocks, count, block_rows, width))
            for w in candidates[1:]:
                got = jnp.where(part == w, windows[w], got)
            return got

        picked = jnp.concatenate([
            pick(0, 1, [REACH_LO]),
            pick(1, 1, list(range(REACH_LO + 1))),
            pick(2, 1, list(range(REACH_LO, REACH_LO + REACH_HI + 1))),
            pick(3, nnz - 3, list(range(REACH_LO + REACH_HI + 1))),
        ], axis=1)
        result = jnp.einsum("bjrc,bjcv->brv", blocks, picked, preferred_element_type=jnp.float32)
        return result.reshape(local_blocks * block_rows, width)

    prev = panel.astype(jnp.float32)
    cur = (apply_operator(panel) - 0.25 * prev) / 2.0
    for degree in range(DEG - 1):
        sent = cur.astype(jnp.bfloat16)
        nxt = 2.0 * (apply_operator(sent) - 0.25 * cur) / 2.0 - prev
        prev = cur
        cur = nxt
    return cur.astype(jnp.bfloat16)


def per_device(vectors, rotation, blocks, columns):
    rotated = jnp.dot(vectors, rotation, preferred_element_type=jnp.float32).astype(jnp.bfloat16)
    panel = lax.all_to_all(rotated, "vec", split_axis=1, concat_axis=0, tiled=True)
    local_blocks = blocks.shape[0]
    n_tiles = local_blocks + REACH_LO + REACH_HI
    first_block = lax.axis_index("row") * local_blocks
    offset = jnp.clip(columns - first_block + REACH_LO - jnp.arange(local_blocks)[:, None], 0, REACH_LO + REACH_HI)
    width = panel.shape[1] // CHUNKS
    outs = [filter_chunk(panel[:, k * width:(k + 1) * width], blocks, offset) for k in range(CHUNKS)]
    return outs[0] if CHUNKS == 1 else jnp.concatenate(outs, axis=1)


def solution(mesh):
    return jax.shard_map(
        per_device,
        mesh=mesh,
        in_specs=(P(("row", "vec"), None), P(), P("row", None, None, None), P("row", None)),
        out_specs=P("row", "vec"),
        check_vma=False,
    )
```

```python
import jax
import jax.numpy as jnp
from jax import lax
from jax.sharding import PartitionSpec as P

DEG = 4
REACH_LO = 6
REACH_HI = 2
CHUNKS = 1


def shift_up(cells, axis):
    count = lax.axis_size(axis)
    return lax.ppermute(cells, axis, [(i, i + 1) for i in range(count - 1)])


def shift_down(cells, axis):
    count = lax.axis_size(axis)
    return lax.ppermute(cells, axis, [(i + 1, i) for i in range(count - 1)])


def swap_halos(state_bf, block_rows):
    count = lax.axis_size("row")
    r = lax.axis_index("row")
    tail = state_bf[state_bf.shape[0] - REACH_LO * block_rows:]
    head = state_bf[: REACH_LO * block_rows]
    even = r % 2 == 0
    pairs_in = []
    pairs_across = []
    for k in range(0, count - 1, 2):
        pairs_in += [(k, k + 1), (k + 1, k)]
    for k in range(1, count - 1, 2):
        pairs_across += [(k, k + 1), (k + 1, k)]
    got_in = lax.ppermute(jnp.where(even, tail, head), "row", pairs_in)
    got_across = lax.ppermute(jnp.where(even, head, tail), "row", pairs_across)
    lo = jnp.where(even, got_across, got_in)
    hi = jnp.where(even, got_in, got_across)[: REACH_HI * block_rows]
    return lo, hi


def filter_chunk(panel, blocks, offset):
    local_blocks, nnz, block_rows, _ = blocks.shape
    width = panel.shape[1]

    def apply_operator(state_bf):
        lo, hi = swap_halos(state_bf, block_rows)
        tiles = jnp.concatenate([lo, state_bf, hi], axis=0).reshape(-1, block_rows, width)
        windows = [tiles[w:w + local_blocks][:, None] for w in range(REACH_LO + REACH_HI + 1)]

        def pick(first, count, candidates):
            part = offset[:, first:first + count, None, None]
            got = jnp.broadcast_to(windows[candidates[0]], (local_blocks, count, block_rows, width))
            for w in candidates[1:]:
                got = jnp.where(part == w, windows[w], got)
            return got

        picked = jnp.concatenate([
            pick(0, 1, [REACH_LO]),
            pick(1, 1, list(range(REACH_LO + 1))),
            pick(2, 1, list(range(REACH_LO, REACH_LO + REACH_HI + 1))),
            pick(3, nnz - 3, list(range(REACH_LO + REACH_HI + 1))),
        ], axis=1)
        result = jnp.einsum("bjrc,bjcv->brv", blocks, picked, preferred_element_type=jnp.float32)
        return result.reshape(local_blocks * block_rows, width)

    prev = panel.astype(jnp.float32)
    cur = (apply_operator(panel) - 0.25 * prev) / 2.0
    for degree in range(DEG - 1):
        sent = cur.astype(jnp.bfloat16)
        nxt = 2.0 * (apply_operator(sent) - 0.25 * cur) / 2.0 - prev
        prev = cur
        cur = nxt
    return cur.astype(jnp.bfloat16)


def per_device(vectors, rotation, blocks, columns):
    rotated = jnp.dot(vectors, rotation, preferred_element_type=jnp.float32).astype(jnp.bfloat16)
    panel = lax.all_to_all(rotated, "vec", split_axis=1, concat_axis=0, tiled=True)
    local_blocks = blocks.shape[0]
    n_tiles = local_blocks + REACH_LO + REACH_HI
    first_block = lax.axis_index("row") * local_blocks
    offset = jnp.clip(columns - first_block + REACH_LO - jnp.arange(local_blocks)[:, None], 0, REACH_LO + REACH_HI)
    width = panel.shape[1] // CHUNKS
    outs = [filter_chunk(panel[:, k * width:(k + 1) * width], blocks, offset) for k in range(CHUNKS)]
    return outs[0] if CHUNKS == 1 else jnp.concatenate(outs, axis=1)


def solution(mesh):
    return jax.shard_map(
        per_device,
        mesh=mesh,
        in_specs=(P(("row", "vec"), None), P(), P("row", None, None, None), P("row", None)),
        out_specs=P("row", "vec"),
        check_vma=False,
    )
```

```python
import jax
import jax.numpy as jnp
from jax import lax
from jax.sharding import PartitionSpec as P

DEG = 4
REACH_LO = 6
REACH_HI = 2


def shift_up(cells, axis):
    count = lax.axis_size(axis)
    return lax.ppermute(cells, axis, [(i, i + 1) for i in range(count - 1)])


def shift_down(cells, axis):
    count = lax.axis_size(axis)
    return lax.ppermute(cells, axis, [(i + 1, i) for i in range(count - 1)])


def filter_chunk(panel, blocks, offset):
    _, nnz, block_rows, _ = blocks.shape
    width = panel.shape[1]
    local_blocks = panel.shape[0] // block_rows - REACH_LO - REACH_HI

    def apply_operator(state_bf, n_rows):
        lo = shift_up(state_bf[(local_blocks - REACH_LO) * block_rows:local_blocks * block_rows], "row")
        tiles = jnp.concatenate([lo, state_bf], axis=0).reshape(-1, block_rows, width)
        windows = [tiles[w:w + n_rows][:, None] for w in range(REACH_LO + REACH_HI + 1)]

        def pick(first, count, candidates):
            part = offset[:n_rows, first:first + count, None, None]
            got = jnp.broadcast_to(windows[candidates[0]], (n_rows, count, block_rows, width))
            for w in candidates[1:]:
                got = jnp.where(part == w, windows[w], got)
            return got

        picked = jnp.concatenate([
            pick(0, 1, [REACH_LO]),
            pick(1, 1, list(range(REACH_LO + 1))),
            pick(2, 1, list(range(REACH_LO, REACH_LO + REACH_HI + 1))),
            pick(3, nnz - 3, list(range(REACH_LO + REACH_HI + 1))),
        ], axis=1)
        result = jnp.einsum("bjrc,bjcv->brv", blocks[:n_rows], picked, preferred_element_type=jnp.float32)
        return result.reshape(n_rows * block_rows, width)

    counts = [local_blocks + REACH_HI * (DEG - 1 - k) for k in range(DEG)]
    n0 = counts[0]
    prev = panel[: n0 * block_rows].astype(jnp.float32)
    cur = (apply_operator(panel, n0) - 0.25 * prev) / 2.0
    for degree in range(DEG - 1):
        n = counts[degree + 1] * block_rows
        sent = cur.astype(jnp.bfloat16)
        nxt = 2.0 * (apply_operator(sent, counts[degree + 1]) - 0.25 * cur[:n]) / 2.0 - prev[:n]
        prev = cur[:n]
        cur = nxt
    return cur.astype(jnp.bfloat16)


def per_device(vectors, rotation, blocks, columns):
    rotated = jnp.dot(vectors, rotation, preferred_element_type=jnp.float32).astype(jnp.bfloat16)
    panel = lax.all_to_all(rotated, "vec", split_axis=1, concat_axis=0, tiled=True)
    local_blocks, _, block_rows, _ = blocks.shape
    extra = REACH_HI * (DEG - 1)
    blocks_ext = jnp.concatenate([blocks, shift_down(blocks[:extra], "row")], axis=0)
    columns_ext = jnp.concatenate([columns, shift_down(columns[:extra], "row")], axis=0)
    panel_ext = jnp.concatenate([panel, shift_down(panel, "row")], axis=0)
    first_block = lax.axis_index("row") * local_blocks
    own = jnp.arange(local_blocks + extra)[:, None]
    offset = jnp.clip(columns_ext - first_block + REACH_LO - own, 0, REACH_LO + REACH_HI)
    return filter_chunk(panel_ext, blocks_ext, offset)


def solution(mesh):
    return jax.shard_map(
        per_device,
        mesh=mesh,
        in_specs=(P(("row", "vec"), None), P(), P("row", None, None, None), P("row", None)),
        out_specs=P("row", "vec"),
        check_vma=False,
    )
```

```python
import jax
import jax.numpy as jnp
from jax import lax
from jax.sharding import PartitionSpec as P

DEG = 4
REACH_LO = 6
REACH_HI = 2
CHUNKS = 1


def shift_up(cells, axis):
    count = lax.axis_size(axis)
    return lax.ppermute(cells, axis, [(i, i + 1) for i in range(count - 1)])


def shift_down(cells, axis):
    count = lax.axis_size(axis)
    return lax.ppermute(cells, axis, [(i + 1, i) for i in range(count - 1)])


def filter_chunk(panel, blocks, offset):
    local_blocks, nnz, block_rows, _ = blocks.shape
    width = panel.shape[1]
    split = REACH_HI

    def product(tiles, first, n_rows):
        windows = [tiles[first + w:first + w + n_rows][:, None] for w in range(REACH_LO + REACH_HI + 1)]

        def pick(entry, count, candidates):
            part = offset[first:first + n_rows, entry:entry + count, None, None]
            got = jnp.broadcast_to(windows[candidates[0]], (n_rows, count, block_rows, width))
            for w in candidates[1:]:
                got = jnp.where(part == w, windows[w], got)
            return got

        picked = jnp.concatenate([
            pick(0, 1, [REACH_LO]),
            pick(1, 1, list(range(REACH_LO + 1))),
            pick(2, 1, list(range(REACH_LO, REACH_LO + REACH_HI + 1))),
            pick(3, nnz - 3, list(range(REACH_LO + REACH_HI + 1))),
        ], axis=1)
        result = jnp.einsum("bjrc,bjcv->brv", blocks[first:first + n_rows], picked, preferred_element_type=jnp.float32)
        return result.reshape(n_rows * block_rows, width)

    def apply_operator(head, rest):
        lo = shift_up(rest, "row")
        hi = shift_down(head, "row")
        part = jnp.concatenate([lo, head, rest], axis=0).reshape(-1, block_rows, width)
        new_head = product(part, 0, split)
        tiles = jnp.concatenate([lo, head, rest, hi], axis=0).reshape(-1, block_rows, width)
        new_rest = product(tiles, split, local_blocks - split)
        return new_head, new_rest

    cut = split * block_rows
    p_head, p_rest = panel[:cut], panel[cut:]
    prev = (p_head.astype(jnp.float32), p_rest.astype(jnp.float32))
    a_head, a_rest = apply_operator(p_head, p_rest)
    cur = ((a_head - 0.25 * prev[0]) / 2.0, (a_rest - 0.25 * prev[1]) / 2.0)
    for degree in range(DEG - 1):
        a_head, a_rest = apply_operator(cur[0].astype(jnp.bfloat16), cur[1].astype(jnp.bfloat16))
        nxt = (
            2.0 * (a_head - 0.25 * cur[0]) / 2.0 - prev[0],
            2.0 * (a_rest - 0.25 * cur[1]) / 2.0 - prev[1],
        )
        prev = cur
        cur = nxt
    return jnp.concatenate([cur[0], cur[1]], axis=0).astype(jnp.bfloat16)


def per_device(vectors, rotation, blocks, columns):
    rotated = jnp.dot(vectors, rotation, preferred_element_type=jnp.float32).astype(jnp.bfloat16)
    panel = lax.all_to_all(rotated, "vec", split_axis=1, concat_axis=0, tiled=True)
    local_blocks = blocks.shape[0]
    n_tiles = local_blocks + REACH_LO + REACH_HI
    first_block = lax.axis_index("row") * local_blocks
    offset = jnp.clip(columns - first_block + REACH_LO - jnp.arange(local_blocks)[:, None], 0, REACH_LO + REACH_HI)
    width = panel.shape[1] // CHUNKS
    outs = [filter_chunk(panel[:, k * width:(k + 1) * width], blocks, offset) for k in range(CHUNKS)]
    return outs[0] if CHUNKS == 1 else jnp.concatenate(outs, axis=1)


def solution(mesh):
    return jax.shard_map(
        per_device,
        mesh=mesh,
        in_specs=(P(("row", "vec"), None), P(), P("row", None, None, None), P("row", None)),
        out_specs=P("row", "vec"),
        check_vma=False,
    )
```

```python
import jax
import jax.numpy as jnp
from jax import lax
from jax.sharding import PartitionSpec as P

DEG = 4
REACH_LO = 6
REACH_HI = 2
CHUNKS = 1


def shift_up(cells, axis):
    count = lax.axis_size(axis)
    return lax.ppermute(cells, axis, [(i, i + 1) for i in range(count - 1)])


def shift_down(cells, axis):
    count = lax.axis_size(axis)
    return lax.ppermute(cells, axis, [(i + 1, i) for i in range(count - 1)])


def swap_halos(state_bf, block_rows):
    count = lax.axis_size("row")
    r = lax.axis_index("row")
    tail = state_bf[state_bf.shape[0] - REACH_LO * block_rows:]
    head = state_bf[: REACH_LO * block_rows]
    even = r % 2 == 0
    pairs_in = []
    pairs_across = []
    for k in range(0, count - 1, 2):
        pairs_in += [(k, k + 1), (k + 1, k)]
    for k in range(1, count - 1, 2):
        pairs_across += [(k, k + 1), (k + 1, k)]
    got_in = lax.ppermute(jnp.where(even, tail, head), "row", pairs_in)
    got_across = lax.ppermute(jnp.where(even, head, tail), "row", pairs_across)
    lo = jnp.where(even, got_across, got_in)
    hi = jnp.where(even, got_in, got_across)[: REACH_HI * block_rows]
    return lo, hi


def filter_chunk(panel, blocks, offset):
    local_blocks, nnz, block_rows, _ = blocks.shape
    width = panel.shape[1]

    def apply_operator(state_bf):
        lo, hi = swap_halos(state_bf, block_rows)
        tiles = jnp.concatenate([lo, state_bf, hi], axis=0).reshape(-1, block_rows, width)
        windows = [tiles[w:w + local_blocks][:, None] for w in range(REACH_LO + REACH_HI + 1)]

        def pick(first, count, candidates):
            part = offset[:, first:first + count, None, None]
            got = jnp.broadcast_to(windows[candidates[0]], (local_blocks, count, block_rows, width))
            for w in candidates[1:]:
                got = jnp.where(part == w, windows[w], got)
            return got

        picked = jnp.concatenate([
            pick(0, 1, [REACH_LO]),
            pick(1, 1, list(range(REACH_LO + 1))),
            pick(2, 1, list(range(REACH_LO, REACH_LO + REACH_HI + 1))),
            pick(3, nnz - 3, list(range(REACH_LO + REACH_HI + 1))),
        ], axis=1)
        result = jnp.einsum("bjrc,bjcv->brv", blocks, picked, preferred_element_type=jnp.float32)
        return result.reshape(local_blocks * block_rows, width)

    prev = panel.astype(jnp.float32)
    cur = (apply_operator(panel) - 0.25 * prev) / 2.0
    for degree in range(DEG - 1):
        sent = cur.astype(jnp.bfloat16)
        nxt = 2.0 * (apply_operator(sent) - 0.25 * cur) / 2.0 - prev
        prev = cur
        cur = nxt
    return cur.astype(jnp.bfloat16)


def per_device(vectors, rotation, blocks, columns):
    rotated_t = lax.dot_general(rotation, vectors, (((0,), (1,)), ((), ())), preferred_element_type=jnp.float32)
    panel_t = lax.all_to_all(rotated_t.astype(jnp.bfloat16), "vec", split_axis=0, concat_axis=1, tiled=True)
    panel = panel_t.T
    local_blocks = blocks.shape[0]
    n_tiles = local_blocks + REACH_LO + REACH_HI
    first_block = lax.axis_index("row") * local_blocks
    offset = jnp.clip(columns - first_block + REACH_LO - jnp.arange(local_blocks)[:, None], 0, REACH_LO + REACH_HI)
    width = panel.shape[1] // CHUNKS
    outs = [filter_chunk(panel[:, k * width:(k + 1) * width], blocks, offset) for k in range(CHUNKS)]
    return outs[0] if CHUNKS == 1 else jnp.concatenate(outs, axis=1)


def solution(mesh):
    return jax.shard_map(
        per_device,
        mesh=mesh,
        in_specs=(P(("row", "vec"), None), P(), P("row", None, None, None), P("row", None)),
        out_specs=P("row", "vec"),
        check_vma=False,
    )
```

```python
import jax
import jax.numpy as jnp
from jax import lax
from jax.sharding import PartitionSpec as P

DEG = 4
REACH_LO = 6
REACH_HI = 2
CHUNKS = 1


def shift_up(cells, axis):
    count = lax.axis_size(axis)
    return lax.ppermute(cells, axis, [(i, i + 1) for i in range(count - 1)])


def shift_down(cells, axis):
    count = lax.axis_size(axis)
    return lax.ppermute(cells, axis, [(i + 1, i) for i in range(count - 1)])


def swap_halos(state_bf, block_rows):
    count = lax.axis_size("row")
    r = lax.axis_index("row")
    tail = state_bf[state_bf.shape[0] - REACH_LO * block_rows:]
    head = state_bf[: REACH_LO * block_rows]
    even = r % 2 == 0
    pairs_in = []
    pairs_across = []
    for k in range(0, count - 1, 2):
        pairs_in += [(k, k + 1), (k + 1, k)]
    for k in range(1, count - 1, 2):
        pairs_across += [(k, k + 1), (k + 1, k)]
    got_in = lax.ppermute(jnp.where(even, tail, head), "row", pairs_in)
    got_across = lax.ppermute(jnp.where(even, head, tail), "row", pairs_across)
    lo = jnp.where(even, got_across, got_in)
    hi = jnp.where(even, got_in, got_across)[: REACH_HI * block_rows]
    return lo, hi


def filter_chunk(panel, blocks, offset):
    local_blocks, nnz, block_rows, _ = blocks.shape
    width = panel.shape[1]

    def apply_operator(state_bf):
        lo, hi = swap_halos(state_bf, block_rows)
        lo_t = lo.reshape(-1, block_rows, width)
        own_t = state_bf.reshape(-1, block_rows, width)
        hi_t = hi.reshape(-1, block_rows, width)

        def window(w):
            parts = [lo_t[w:], own_t[:max(w + local_blocks - REACH_LO, 0)]] if w < REACH_LO else [own_t[w - REACH_LO:]]
            if w + local_blocks > REACH_LO + local_blocks:
                parts.append(hi_t[:w + local_blocks - REACH_LO - local_blocks])
            parts = [p for p in parts if p.shape[0] > 0]
            return jnp.concatenate(parts, axis=0)[:, None]

        windows = [window(w) for w in range(REACH_LO + REACH_HI + 1)]

        def pick(first, count, candidates):
            part = offset[:, first:first + count, None, None]
            got = jnp.broadcast_to(windows[candidates[0]], (local_blocks, count, block_rows, width))
            for w in candidates[1:]:
                got = jnp.where(part == w, windows[w], got)
            return got

        picked = jnp.concatenate([
            pick(0, 1, [REACH_LO]),
            pick(1, 1, list(range(REACH_LO + 1))),
            pick(2, 1, list(range(REACH_LO, REACH_LO + REACH_HI + 1))),
            pick(3, nnz - 3, list(range(REACH_LO + REACH_HI + 1))),
        ], axis=1)
        result = jnp.einsum("bjrc,bjcv->brv", blocks, picked, preferred_element_type=jnp.float32)
        return result.reshape(local_blocks * block_rows, width)

    prev = panel.astype(jnp.float32)
    cur = (apply_operator(panel) - 0.25 * prev) / 2.0
    for degree in range(DEG - 1):
        sent = cur.astype(jnp.bfloat16)
        nxt = 2.0 * (apply_operator(sent) - 0.25 * cur) / 2.0 - prev
        prev = cur
        cur = nxt
    return cur.astype(jnp.bfloat16)


def per_device(vectors, rotation, blocks, columns):
    rotated_t = lax.dot_general(rotation, vectors, (((0,), (1,)), ((), ())), preferred_element_type=jnp.float32)
    panel_t = lax.all_to_all(rotated_t.astype(jnp.bfloat16), "vec", split_axis=0, concat_axis=1, tiled=True)
    panel = panel_t.T
    local_blocks = blocks.shape[0]
    n_tiles = local_blocks + REACH_LO + REACH_HI
    first_block = lax.axis_index("row") * local_blocks
    offset = jnp.clip(columns - first_block + REACH_LO - jnp.arange(local_blocks)[:, None], 0, REACH_LO + REACH_HI)
    width = panel.shape[1] // CHUNKS
    outs = [filter_chunk(panel[:, k * width:(k + 1) * width], blocks, offset) for k in range(CHUNKS)]
    return outs[0] if CHUNKS == 1 else jnp.concatenate(outs, axis=1)


def solution(mesh):
    return jax.shard_map(
        per_device,
        mesh=mesh,
        in_specs=(P(("row", "vec"), None), P(), P("row", None, None, None), P("row", None)),
        out_specs=P("row", "vec"),
        check_vma=False,
    )
```

```python
import jax
import jax.numpy as jnp
from jax import lax
from jax.sharding import PartitionSpec as P

DEG = 4
REACH_LO = 6
REACH_HI = 2
CHUNKS = 1


def shift_up(cells, axis):
    count = lax.axis_size(axis)
    return lax.ppermute(cells, axis, [(i, i + 1) for i in range(count - 1)])


def shift_down(cells, axis):
    count = lax.axis_size(axis)
    return lax.ppermute(cells, axis, [(i + 1, i) for i in range(count - 1)])


def filter_chunk(panel, blocks, offset):
    local_blocks, nnz, block_rows, _ = blocks.shape
    width = panel.shape[1]

    def apply_operator(state_bf):
        lo = shift_up(state_bf[state_bf.shape[0] - REACH_LO * block_rows:], "row")
        hi = shift_down(state_bf[: REACH_HI * block_rows], "row")
        tiles = jnp.concatenate([lo, state_bf, hi], axis=0).reshape(-1, block_rows, width)
        windows = [tiles[w:w + local_blocks][:, None] for w in range(REACH_LO + REACH_HI + 1)]

        def pick(first, count, candidates):
            part = offset[:, first:first + count, None, None]
            got = jnp.broadcast_to(windows[candidates[0]], (local_blocks, count, block_rows, width))
            for w in candidates[1:]:
                got = jnp.where(part == w, windows[w], got)
            return got

        picked = jnp.concatenate([
            pick(0, 1, [REACH_LO]),
            pick(1, 1, list(range(REACH_LO + 1))),
            pick(2, 1, list(range(REACH_LO, REACH_LO + REACH_HI + 1))),
            pick(3, nnz - 3, list(range(REACH_LO + REACH_HI + 1))),
        ], axis=1)
        result = jnp.einsum("bjrc,bjcv->brv", blocks, picked, preferred_element_type=jnp.float32)
        return result.reshape(local_blocks * block_rows, width)

    prev = panel.astype(jnp.float32)
    cur = (apply_operator(panel) - 0.25 * prev) / 2.0
    for degree in range(DEG - 1):
        sent = cur.astype(jnp.bfloat16)
        nxt = 2.0 * (apply_operator(sent) - 0.25 * cur) / 2.0 - prev
        prev = cur
        cur = nxt
    return cur.astype(jnp.bfloat16)


def per_device(vectors, rotation, blocks, columns):
    rotated_t = lax.dot_general(rotation, vectors, (((0,), (1,)), ((), ())), preferred_element_type=jnp.float32)
    panel_t = lax.all_to_all(rotated_t.astype(jnp.bfloat16), "vec", split_axis=0, concat_axis=1, tiled=True)
    panel = panel_t.T
    local_blocks = blocks.shape[0]
    n_tiles = local_blocks + REACH_LO + REACH_HI
    first_block = lax.axis_index("row") * local_blocks
    offset = jnp.clip(columns - first_block + REACH_LO - jnp.arange(local_blocks)[:, None], 0, REACH_LO + REACH_HI)
    width = panel.shape[1] // CHUNKS
    outs = [filter_chunk(panel[:, k * width:(k + 1) * width], blocks, offset) for k in range(CHUNKS)]
    return outs[0] if CHUNKS == 1 else jnp.concatenate(outs, axis=1)


def solution(mesh):
    return jax.shard_map(
        per_device,
        mesh=mesh,
        in_specs=(P(("row", "vec"), None), P(), P("row", None, None, None), P("row", None)),
        out_specs=P("row", "vec"),
        check_vma=False,
    )
```
